256 devices in a mesh: section: 8 (over y, core), seq: 8 (over z), chan: 4 (over x).
Axes of the slice: x: 4, y: 4, z: 8, core: 2. Of those that a mesh axis runs over, the one named last changes fastest.
Arguments:
- layer_rows: bfloat16 [8, 8192, 8192], P('section', 'seq', 'chan'), may hold values from -6 to 6
- in_weight: bfloat16 [8, 8192, 768], P('section', 'chan'), may hold values from -0.0625 to 0.0625
- long_filter: float32 [8, 8192, 256], P('section', ('seq', 'chan')), may hold values from -2 to 2, as said below
- skip_gain: float32 [8, 256], P('section'), may hold values from -4 to 4
Outputs:
- gated_out: bfloat16 [8, 8192, 256], P('section', ('seq', 'chan'))
The draws below stay inside these ranges and needn't reach their ends.
Inputs may be any that keep to these rules, and one draw needn't show every extreme that they name: `long_filter`: filter taps of each channel.
All inputs are finite; a program needn't handle non-finite values.
Results may differ from the reference program's by a relative error of at most 0.0064.
Values may be sent and summed in bfloat16 or wider, within the bound.
No kernel may reach another device: no remote copies, remote signals or barrier semaphores. Data moves between devices by JAX's collectives and lax.ppermute only.
A program may use at most 64 MiB of HBM per device.

```python
import math
import jax
import jax.numpy as jnp

D = 8192
C = 256
SEQ_LEN = 8192
N_SECTION = 8


def draw_long_filter(key, part):
    noise_key, rate_key = jax.random.split(key)
    positions = jnp.arange(SEQ_LEN, dtype=jnp.float32)[None, :, None]
    noise_values = jnp.clip(jax.random.normal(noise_key, (N_SECTION, SEQ_LEN, C), jnp.float32), -6.0, 6.0)
    rate_floor = math.log(0.25 / SEQ_LEN)
    rate_ceiling = math.log(1.0 / 30.0)
    rates = jnp.exp(jax.random.uniform(rate_key, (N_SECTION, 1, C), jnp.float32, rate_floor, rate_ceiling))
    return noise_values * jnp.sqrt(2.0 * rates) * jnp.exp(-rates * positions)


def level_of(key, dims, cuts, least, high):
    loudness, own = 1.0, jax.random.fold_in(key, 6)
    for position, blocks in cuts:
        steps = jnp.exp(jax.random.uniform(jax.random.fold_in(own, position), (blocks,), jnp.float32, least / len(cuts), high / len(cuts)))
        loudness = loudness * jnp.repeat(steps, dims[position] // blocks).reshape([-1 if axis == position else 1 for axis in range(len(dims))])
    return loudness


def bell_draw(own_key, extent, spread, bound, shards=(), kind=jnp.bfloat16):
    result = jax.random.normal(own_key, extent, jnp.float32) * spread
    if len(shards) > 0:
        result = level_of(own_key, extent, shards, -0.22, 0.18) * result
    return jnp.clip(result, min=-bound, max=bound).astype(kind)


def setup_inputs(seed: int = 0) -> dict:
    splits = jax.random.split(jax.random.key(seed), 5)
    return {
        "layer_rows": bell_draw(splits[0], (N_SECTION, SEQ_LEN, D), 1.0, 6.0, ((0, 8), (1, 8), (2, 4))),
        "in_weight": bell_draw(splits[1], (N_SECTION, D, 3 * C), D ** -0.5, 0.0625, ((0, 8), (1, 4))),
        "long_filter": draw_long_filter(jax.random.fold_in(splits[4], 71), 0),
        "skip_gain": bell_draw(splits[3], (N_SECTION, C), 1.0, 4.0, ((0, 8),), jnp.float32),
    }


def reference(layer_rows, in_weight, long_filter, skip_gain):
    results = []
    for section_index in range(N_SECTION):
        source = layer_rows[(section_index - 1) % N_SECTION]
        mixed = jnp.dot(source, in_weight[section_index], preferred_element_type=jnp.float32).astype(jnp.bfloat16)
        queries = mixed[:, :C].astype(jnp.float32)
        keys = mixed[:, C:2 * C].astype(jnp.float32)
        values_part = mixed[:, 2 * C:].astype(jnp.float32)
        signal = keys * values_part
        spectrum = jnp.fft.rfft(signal, n=2 * SEQ_LEN, axis=0) * jnp.fft.rfft(long_filter[section_index], n=2 * SEQ_LEN, axis=0)
        conv = jnp.fft.irfft(spectrum, n=2 * SEQ_LEN, axis=0)[:SEQ_LEN]
        gated = queries * (conv + skip_gain[section_index][None, :] * signal)
        results.append(gated.astype(jnp.bfloat16))
    return jnp.stack(results)
```

```python
import jax
import jax.numpy as jnp
from jax import lax
from jax.sharding import PartitionSpec as P


def from_behind(value, axis, steps):
    count = lax.axis_size(axis)
    pairs = [(source, (source + steps) % count) for source in range(count)]
    return lax.ppermute(value, axis, pairs)


def body(layer_rows, in_weight, long_filter, skip_gain):
    n_chan = lax.axis_size("chan")
    n_seq = lax.axis_size("seq")
    n_pos = n_chan * n_seq
    width = long_filter.shape[2]
    block_rows = long_filter.shape[1]
    seq_rows = layer_rows.shape[1]
    seq_len = block_rows * n_pos
    fft_length = 2 * seq_len
    chan_width = width // n_chan
    own = chan_width // n_seq
    q_index = lax.axis_index("seq")
    c_index = lax.axis_index("chan")

    taps = long_filter[0].reshape(block_rows, n_chan, n_seq, own)
    taps = taps.transpose(2, 1, 3, 0).reshape(n_pos, own, block_rows)
    taps = lax.all_to_all(taps, ("seq", "chan"), 0, 0, tiled=True)
    taps = taps.reshape(n_pos, own, block_rows).transpose(1, 0, 2).reshape(own, seq_len)
    taps_freq = jnp.fft.rfft(taps, n=fft_length, axis=-1)

    weight = in_weight[0].reshape(-1, 3, n_chan, chan_width)
    weight = weight.transpose(0, 2, 1, 3).reshape(-1, 3 * width)

    source = from_behind(layer_rows, "section", 1)[0]
    partial = jnp.einsum("fn,rf->nr", weight, source, preferred_element_type=jnp.float32)
    summed = lax.psum_scatter(partial, "chan", scatter_dimension=0, tiled=True)
    mixed = summed.astype(jnp.bfloat16).reshape(3, n_seq, own, seq_rows)
    mixed = mixed.transpose(1, 0, 2, 3)
    mixed = lax.all_to_all(mixed, "seq", 0, 0, tiled=True)
    mixed = mixed.reshape(n_seq, 3, own, seq_rows).transpose(1, 2, 0, 3).reshape(3, own, seq_len)
    queries = mixed[0].astype(jnp.float32)
    signal = mixed[1].astype(jnp.float32) * mixed[2].astype(jnp.float32)

    spectrum = jnp.fft.rfft(signal, n=fft_length, axis=-1) * taps_freq
    conv = jnp.fft.irfft(spectrum, n=fft_length, axis=-1)[:, :seq_len]
    gain = lax.dynamic_slice_in_dim(skip_gain[0], c_index * chan_width + q_index * own, own)
    gated = (queries * (conv + gain[:, None] * signal)).astype(jnp.bfloat16)

    gated = gated.reshape(own, n_pos, block_rows).transpose(1, 0, 2)
    gated = lax.all_to_all(gated, ("seq", "chan"), 0, 0, tiled=True)
    gated = gated.reshape(n_seq, n_chan, own, block_rows).transpose(3, 1, 0, 2)
    return gated.reshape(block_rows, width)[None]


def solution(mesh):
    in_specs = (
        P("section", "seq", "chan"),
        P("section", "chan", None),
        P("section", ("seq", "chan"), None),
        P("section", None),
    )
    out_specs = P("section", ("seq", "chan"), None)
    return jax.shard_map(body, mesh=mesh, in_specs=in_specs, out_specs=out_specs, check_vma=False)
```

```python
import jax
import jax.numpy as jnp
from jax import lax
from jax.sharding import PartitionSpec as P


CHUNKS = 4


def from_behind(value, axis, steps):
    count = lax.axis_size(axis)
    pairs = [(source, (source + steps) % count) for source in range(count)]
    return lax.ppermute(value, axis, pairs)


def body(layer_rows, in_weight, long_filter, skip_gain):
    n_chan = lax.axis_size("chan")
    n_seq = lax.axis_size("seq")
    n_pos = n_chan * n_seq
    width = long_filter.shape[2]
    block_rows = long_filter.shape[1]
    seq_rows = layer_rows.shape[1]
    seq_len = block_rows * n_pos
    fft_length = 2 * seq_len
    chan_width = width // n_chan
    own = chan_width // n_seq
    q_index = lax.axis_index("seq")
    c_index = lax.axis_index("chan")

    taps = long_filter[0].reshape(block_rows, n_chan, n_seq, own)
    taps = taps.transpose(2, 1, 3, 0).reshape(n_pos, own, block_rows)
    taps = lax.all_to_all(taps, ("seq", "chan"), 0, 0, tiled=True)
    taps = taps.reshape(n_pos, own, block_rows).transpose(1, 0, 2).reshape(own, seq_len)
    taps_freq = jnp.fft.rfft(taps, n=fft_length, axis=-1)

    weight = in_weight[0].reshape(-1, 3, n_chan, chan_width)
    weight = weight.transpose(0, 2, 1, 3).reshape(-1, 3 * width)

    pieces = []
    chunk_rows = seq_rows // CHUNKS
    for chunk in range(CHUNKS):
        rows = layer_rows[:, chunk * chunk_rows : (chunk + 1) * chunk_rows]
        source = from_behind(rows, "section", 1)[0]
        partial = jnp.einsum("fn,rf->nr", weight, source, preferred_element_type=jnp.float32)
        summed = lax.psum_scatter(partial, "chan", scatter_dimension=0, tiled=True)
        pieces.append(summed.astype(jnp.bfloat16))
    mixed = jnp.concatenate(pieces, axis=1).reshape(3, n_seq, own, seq_rows)
    mixed = mixed.transpose(1, 0, 2, 3)
    mixed = lax.all_to_all(mixed, "seq", 0, 0, tiled=True)
    mixed = mixed.reshape(n_seq, 3, own, seq_rows).transpose(1, 2, 0, 3).reshape(3, own, seq_len)
    queries = mixed[0].astype(jnp.float32)
    signal = mixed[1].astype(jnp.float32) * mixed[2].astype(jnp.float32)

    spectrum = jnp.fft.rfft(signal, n=fft_length, axis=-1) * taps_freq
    conv = jnp.fft.irfft(spectrum, n=fft_length, axis=-1)[:, :seq_len]
    gain = lax.dynamic_slice_in_dim(skip_gain[0], c_index * chan_width + q_index * own, own)
    gated = (queries * (conv + gain[:, None] * signal)).astype(jnp.bfloat16)

    gated = gated.reshape(own, n_pos, block_rows).transpose(1, 0, 2)
    gated = lax.all_to_all(gated, ("seq", "chan"), 0, 0, tiled=True)
    gated = gated.reshape(n_seq, n_chan, own, block_rows).transpose(3, 1, 0, 2)
    return gated.reshape(block_rows, width)[None]


def solution(mesh):
    in_specs = (
        P("section", "seq", "chan"),
        P("section", "chan", None),
        P("section", ("seq", "chan"), None),
        P("section", None),
    )
    out_specs = P("section", ("seq", "chan"), None)
    return jax.shard_map(body, mesh=mesh, in_specs=in_specs, out_specs=out_specs, check_vma=False)
```

```python
import math

import numpy as np
import jax
import jax.numpy as jnp
from jax import lax
from jax.sharding import PartitionSpec as P


CHUNKS = 2
HI = lax.Precision.HIGHEST


def dft_tables(seq_len):
    fft_length = 2 * seq_len
    side = int(round(math.sqrt(fft_length)))
    half = seq_len // side
    k = np.arange(side)
    m = np.arange(half)
    outer = 2 * np.pi * np.outer(k, m) / side
    fine = 2 * np.pi * (np.outer(k, k) % side) / side
    twist = 2 * np.pi * (np.outer(k, k) % fft_length) / fft_length
    f32 = lambda a: jnp.asarray(a, dtype=jnp.float32)
    return dict(
        side=side, half=half,
        a_cos=f32(np.cos(outer)), a_sin=f32(np.sin(outer)),
        c_cos=f32(np.cos(fine)), c_sin=f32(np.sin(fine)),
        t_cos=f32(np.cos(twist)), t_sin=f32(np.sin(twist)),
        i_cos=f32(np.cos(outer) / fft_length), i_sin=f32(np.sin(outer) / fft_length),
    )


def forward(x, t):
    c = x.shape[0]
    x = x.reshape(c, t["half"], t["side"])
    y_re = jnp.einsum("km,cmr->ckr", t["a_cos"], x, precision=HI)
    y_im = -jnp.einsum("km,cmr->ckr", t["a_sin"], x, precision=HI)
    z_re = y_re * t["t_cos"] + y_im * t["t_sin"]
    z_im = y_im * t["t_cos"] - y_re * t["t_sin"]
    s_re = jnp.einsum("ckr,rj->ckj", z_re, t["c_cos"], precision=HI) + jnp.einsum("ckr,rj->ckj", z_im, t["c_sin"], precision=HI)
    s_im = jnp.einsum("ckr,rj->ckj", z_im, t["c_cos"], precision=HI) - jnp.einsum("ckr,rj->ckj", z_re, t["c_sin"], precision=HI)
    return s_re, s_im


def inverse(p_re, p_im, t):
    c = p_re.shape[0]
    u_re = jnp.einsum("ckj,jr->ckr", p_re, t["c_cos"], precision=HI) - jnp.einsum("ckj,jr->ckr", p_im, t["c_sin"], precision=HI)
    u_im = jnp.einsum("ckj,jr->ckr", p_im, t["c_cos"], precision=HI) + jnp.einsum("ckj,jr->ckr", p_re, t["c_sin"], precision=HI)
    v_re = u_re * t["t_cos"] - u_im * t["t_sin"]
    v_im = u_im * t["t_cos"] + u_re * t["t_sin"]
    out = jnp.einsum("km,ckr->cmr", t["i_cos"], v_re, precision=HI) - jnp.einsum("km,ckr->cmr", t["i_sin"], v_im, precision=HI)
    return out.reshape(c, -1)


def from_behind(value, axis, steps):
    count = lax.axis_size(axis)
    pairs = [(source, (source + steps) % count) for source in range(count)]
    return lax.ppermute(value, axis, pairs)


def body(layer_rows, in_weight, long_filter, skip_gain):
    n_chan = lax.axis_size("chan")
    n_seq = lax.axis_size("seq")
    n_pos = n_chan * n_seq
    width = long_filter.shape[2]
    block_rows = long_filter.shape[1]
    seq_rows = layer_rows.shape[1]
    seq_len = block_rows * n_pos
    chan_width = width // n_chan
    own = chan_width // n_seq
    q_index = lax.axis_index("seq")
    c_index = lax.axis_index("chan")

    tables = dft_tables(seq_len)

    taps = long_filter[0].reshape(block_rows, n_chan, n_seq, own)
    taps = taps.transpose(2, 1, 3, 0).reshape(n_pos, own, block_rows)
    taps = lax.all_to_all(taps, ("seq", "chan"), 0, 0, tiled=True)
    taps = taps.reshape(n_pos, own, block_rows).transpose(1, 0, 2).reshape(own, seq_len)
    taps_re, taps_im = forward(taps, tables)

    weight = in_weight[0].reshape(-1, 3, n_chan, chan_width)
    weight = weight.transpose(0, 2, 1, 3).reshape(-1, 3 * width)

    pieces = []
    chunk_rows = seq_rows // CHUNKS
    for chunk in range(CHUNKS):
        rows = layer_rows[:, chunk * chunk_rows : (chunk + 1) * chunk_rows]
        source = from_behind(rows, "section", 1)[0]
        partial = jnp.einsum("fn,rf->nr", weight, source, preferred_element_type=jnp.float32)
        summed = lax.psum_scatter(partial, "chan", scatter_dimension=0, tiled=True)
        pieces.append(summed.astype(jnp.bfloat16))
    mixed = jnp.concatenate(pieces, axis=1).reshape(3, n_seq, own, seq_rows)
    mixed = mixed.transpose(1, 0, 2, 3)
    mixed = lax.all_to_all(mixed, "seq", 0, 0, tiled=True)
    mixed = mixed.reshape(n_seq, 3, own, seq_rows).transpose(1, 2, 0, 3).reshape(3, own, seq_len)
    queries = mixed[0].astype(jnp.float32)
    signal = mixed[1].astype(jnp.float32) * mixed[2].astype(jnp.float32)

    sig_re, sig_im = forward(signal, tables)
    prod_re = sig_re * taps_re - sig_im * taps_im
    prod_im = sig_re * taps_im + sig_im * taps_re
    conv = inverse(prod_re, prod_im, tables)
    gain = lax.dynamic_slice_in_dim(skip_gain[0], c_index * chan_width + q_index * own, own)
    gated = (queries * (conv + gain[:, None] * signal)).astype(jnp.bfloat16)

    gated = gated.reshape(own, n_pos, block_rows).transpose(1, 0, 2)
    gated = lax.all_to_all(gated, ("seq", "chan"), 0, 0, tiled=True)
    gated = gated.reshape(n_seq, n_chan, own, block_rows).transpose(3, 1, 0, 2)
    return gated.reshape(block_rows, width)[None]


def solution(mesh):
    in_specs = (
        P("section", "seq", "chan"),
        P("section", "chan", None),
        P("section", ("seq", "chan"), None),
        P("section", None),
    )
    out_specs = P("section", ("seq", "chan"), None)
    return jax.shard_map(body, mesh=mesh, in_specs=in_specs, out_specs=out_specs, check_vma=False)
```

```python
import math

import numpy as np
import jax
import jax.numpy as jnp
from jax import lax
from jax.sharding import PartitionSpec as P


CHUNKS = 2
HI = lax.Precision.HIGH


def dft_tables(seq_len):
    fft_length = 2 * seq_len
    side = int(round(math.sqrt(fft_length)))
    half = seq_len // side
    k = np.arange(side)
    m = np.arange(half)
    outer = 2 * np.pi * np.outer(k, m) / side
    fine = 2 * np.pi * (np.outer(k, k) % side) / side
    twist = 2 * np.pi * (np.outer(k, k) % fft_length) / fft_length
    f32 = lambda a: jnp.asarray(a, dtype=jnp.float32)
    return dict(
        side=side, half=half,
        a_cos=f32(np.cos(outer)), a_sin=f32(np.sin(outer)),
        c_cos=f32(np.cos(fine)), c_sin=f32(np.sin(fine)),
        t_cos=f32(np.cos(twist)), t_sin=f32(np.sin(twist)),
        i_cos=f32(np.cos(outer) / fft_length), i_sin=f32(np.sin(outer) / fft_length),
    )


def forward(x, t):
    c = x.shape[0]
    x = x.reshape(c, t["half"], t["side"])
    y_re = jnp.einsum("km,cmr->ckr", t["a_cos"], x, precision=HI)
    y_im = -jnp.einsum("km,cmr->ckr", t["a_sin"], x, precision=HI)
    z_re = y_re * t["t_cos"] + y_im * t["t_sin"]
    z_im = y_im * t["t_cos"] - y_re * t["t_sin"]
    s_re = jnp.einsum("ckr,rj->ckj", z_re, t["c_cos"], precision=HI) + jnp.einsum("ckr,rj->ckj", z_im, t["c_sin"], precision=HI)
    s_im = jnp.einsum("ckr,rj->ckj", z_im, t["c_cos"], precision=HI) - jnp.einsum("ckr,rj->ckj", z_re, t["c_sin"], precision=HI)
    return s_re, s_im


def inverse(p_re, p_im, t):
    c = p_re.shape[0]
    u_re = jnp.einsum("ckj,jr->ckr", p_re, t["c_cos"], precision=HI) - jnp.einsum("ckj,jr->ckr", p_im, t["c_sin"], precision=HI)
    u_im = jnp.einsum("ckj,jr->ckr", p_im, t["c_cos"], precision=HI) + jnp.einsum("ckj,jr->ckr", p_re, t["c_sin"], precision=HI)
    v_re = u_re * t["t_cos"] - u_im * t["t_sin"]
    v_im = u_im * t["t_cos"] + u_re * t["t_sin"]
    out = jnp.einsum("km,ckr->cmr", t["i_cos"], v_re, precision=HI) - jnp.einsum("km,ckr->cmr", t["i_sin"], v_im, precision=HI)
    return out.reshape(c, -1)


def from_behind(value, axis, steps):
    count = lax.axis_size(axis)
    pairs = [(source, (source + steps) % count) for source in range(count)]
    return lax.ppermute(value, axis, pairs)


def body(layer_rows, in_weight, long_filter, skip_gain):
    n_chan = lax.axis_size("chan")
    n_seq = lax.axis_size("seq")
    n_pos = n_chan * n_seq
    width = long_filter.shape[2]
    block_rows = long_filter.shape[1]
    seq_rows = layer_rows.shape[1]
    seq_len = block_rows * n_pos
    chan_width = width // n_chan
    own = chan_width // n_seq
    q_index = lax.axis_index("seq")
    c_index = lax.axis_index("chan")

    tables = dft_tables(seq_len)

    taps = long_filter[0].reshape(block_rows, n_chan, n_seq, own)
    taps = taps.transpose(2, 1, 3, 0).reshape(n_pos, own, block_rows)
    taps = lax.all_to_all(taps, ("seq", "chan"), 0, 0, tiled=True)
    taps = taps.reshape(n_pos, own, block_rows).transpose(1, 0, 2).reshape(own, seq_len)
    taps_re, taps_im = forward(taps, tables)

    weight = in_weight[0].reshape(-1, 3, n_chan, chan_width)
    weight = weight.transpose(0, 2, 1, 3)
    rows = layer_rows[0]
    pieces = []
    piece = chan_width // CHUNKS
    for chunk in range(CHUNKS):
        part = weight[:, :, :, chunk * piece : (chunk + 1) * piece].reshape(-1, 3 * n_chan * piece)
        part = from_behind(part, "section", -1)
        partial = jnp.einsum("fn,rf->nr", part, rows, preferred_element_type=jnp.float32)
        summed = lax.psum_scatter(partial, "chan", scatter_dimension=0, tiled=True)
        summed = summed.astype(jnp.bfloat16).reshape(3, piece, seq_rows)
        pieces.append(from_behind(summed, "section", 1))
    mixed = jnp.concatenate(pieces, axis=1).reshape(3, n_seq, own, seq_rows)
    mixed = mixed.transpose(1, 0, 2, 3)
    mixed = lax.all_to_all(mixed, "seq", 0, 0, tiled=True)
    mixed = mixed.reshape(n_seq, 3, own, seq_rows).transpose(1, 2, 0, 3).reshape(3, own, seq_len)
    queries = mixed[0].astype(jnp.float32)
    signal = mixed[1].astype(jnp.float32) * mixed[2].astype(jnp.float32)

    sig_re, sig_im = forward(signal, tables)
    prod_re = sig_re * taps_re - sig_im * taps_im
    prod_im = sig_re * taps_im + sig_im * taps_re
    conv = inverse(prod_re, prod_im, tables)
    gain = lax.dynamic_slice_in_dim(skip_gain[0], c_index * chan_width + q_index * own, own)
    gated = (queries * (conv + gain[:, None] * signal)).astype(jnp.bfloat16)

    gated = gated.reshape(own, n_pos, block_rows).transpose(1, 0, 2)
    gated = lax.all_to_all(gated, ("seq", "chan"), 0, 0, tiled=True)
    gated = gated.reshape(n_seq, n_chan, own, block_rows).transpose(3, 1, 0, 2)
    return gated.reshape(block_rows, width)[None]


def solution(mesh):
    in_specs = (
        P("section", "seq", "chan"),
        P("section", "chan", None),
        P("section", ("seq", "chan"), None),
        P("section", None),
    )
    out_specs = P("section", ("seq", "chan"), None)
    return jax.shard_map(body, mesh=mesh, in_specs=in_specs, out_specs=out_specs, check_vma=False)
```

```python
import math

import numpy as np
import jax
import jax.numpy as jnp
from jax import lax
from jax.sharding import PartitionSpec as P


CHUNKS = 2
HI = lax.Precision.HIGH


def dft_tables(seq_len):
    fft_length = 2 * seq_len
    side = int(round(math.sqrt(fft_length)))
    half = seq_len // side
    k = np.arange(side)
    m = np.arange(half)
    outer = 2 * np.pi * np.outer(k, m) / side
    fine = 2 * np.pi * (np.outer(k, k) % side) / side
    twist = 2 * np.pi * (np.outer(k, k) % fft_length) / fft_length
    f32 = lambda a: jnp.asarray(a, dtype=jnp.float32)
    return dict(
        side=side, half=half,
        a_cos=f32(np.cos(outer)), a_sin=f32(np.sin(outer)),
        c_cos=f32(np.cos(fine)), c_sin=f32(np.sin(fine)),
        t_cos=f32(np.cos(twist)), t_sin=f32(np.sin(twist)),
        i_cos=f32(np.cos(outer) / fft_length), i_sin=f32(np.sin(outer) / fft_length),
    )


def forward(x, t):
    c = x.shape[0]
    x = x.reshape(c, t["half"], t["side"])
    y_re = jnp.einsum("km,cmr->ckr", t["a_cos"], x, precision=HI)
    y_im = -jnp.einsum("km,cmr->ckr", t["a_sin"], x, precision=HI)
    z_re = y_re * t["t_cos"] + y_im * t["t_sin"]
    z_im = y_im * t["t_cos"] - y_re * t["t_sin"]
    s_re = jnp.einsum("ckr,rj->ckj", z_re, t["c_cos"], precision=HI) + jnp.einsum("ckr,rj->ckj", z_im, t["c_sin"], precision=HI)
    s_im = jnp.einsum("ckr,rj->ckj", z_im, t["c_cos"], precision=HI) - jnp.einsum("ckr,rj->ckj", z_re, t["c_sin"], precision=HI)
    return s_re, s_im


def inverse(p_re, p_im, t):
    c = p_re.shape[0]
    u_re = jnp.einsum("ckj,jr->ckr", p_re, t["c_cos"], precision=HI) - jnp.einsum("ckj,jr->ckr", p_im, t["c_sin"], precision=HI)
    u_im = jnp.einsum("ckj,jr->ckr", p_im, t["c_cos"], precision=HI) + jnp.einsum("ckj,jr->ckr", p_re, t["c_sin"], precision=HI)
    v_re = u_re * t["t_cos"] - u_im * t["t_sin"]
    v_im = u_im * t["t_cos"] + u_re * t["t_sin"]
    out = jnp.einsum("km,ckr->cmr", t["i_cos"], v_re, precision=HI) - jnp.einsum("km,ckr->cmr", t["i_sin"], v_im, precision=HI)
    return out.reshape(c, -1)


def from_behind(value, axis, steps):
    count = lax.axis_size(axis)
    pairs = [(source, (source + steps) % count) for source in range(count)]
    return lax.ppermute(value, axis, pairs)


def to_owner(value, shift):
    sections = lax.axis_size("section")
    count = lax.axis_size("seq")
    pairs = [
        (s * count + q, ((s + 1) % sections) * count + (q + shift) % count)
        for s in range(sections)
        for q in range(count)
    ]
    return lax.ppermute(value, ("section", "seq"), pairs)


def body(layer_rows, in_weight, long_filter, skip_gain):
    n_chan = lax.axis_size("chan")
    n_seq = lax.axis_size("seq")
    n_pos = n_chan * n_seq
    width = long_filter.shape[2]
    block_rows = long_filter.shape[1]
    seq_rows = layer_rows.shape[1]
    seq_len = block_rows * n_pos
    chan_width = width // n_chan
    own = chan_width // n_seq
    q_index = lax.axis_index("seq")
    c_index = lax.axis_index("chan")

    tables = dft_tables(seq_len)

    taps = long_filter[0].reshape(block_rows, n_chan, n_seq, own)
    taps = taps.transpose(2, 1, 3, 0).reshape(n_pos, own, block_rows)
    taps = lax.all_to_all(taps, ("seq", "chan"), 0, 0, tiled=True)
    taps = taps.reshape(n_pos, own, block_rows).transpose(1, 0, 2).reshape(own, seq_len)
    taps_re, taps_im = forward(taps, tables)

    weight = in_weight[0].reshape(-1, 3, n_chan, n_seq, own)
    weight = jnp.concatenate([weight, weight], axis=3)
    weight = lax.dynamic_slice_in_dim(weight, q_index, n_seq, axis=3)
    weight = weight.transpose(0, 2, 1, 3, 4)
    rows = layer_rows[0]
    arrived = [None] * n_seq
    shifts = n_seq // CHUNKS
    for chunk in range(CHUNKS):
        part = weight[:, :, :, chunk * shifts : (chunk + 1) * shifts].reshape(-1, 3 * n_chan * shifts * own)
        part = from_behind(part, "section", -1)
        partial = jnp.einsum("fn,rf->nr", part, rows, preferred_element_type=jnp.float32)
        summed = lax.psum_scatter(partial, "chan", scatter_dimension=0, tiled=True)
        summed = summed.astype(jnp.bfloat16).reshape(3, shifts, own, seq_rows)
        for step in range(shifts):
            shift = chunk * shifts + step
            arrived[shift] = to_owner(summed[:, step], shift)
    stacked = jnp.stack(arrived[::-1])
    stacked = jnp.concatenate([stacked, stacked], axis=0)
    mixed = lax.dynamic_slice_in_dim(stacked, n_seq - 1 - q_index, n_seq, axis=0)
    mixed = mixed.transpose(1, 2, 0, 3).reshape(3, own, seq_len)
    queries = mixed[0].astype(jnp.float32)
    signal = mixed[1].astype(jnp.float32) * mixed[2].astype(jnp.float32)

    sig_re, sig_im = forward(signal, tables)
    prod_re = sig_re * taps_re - sig_im * taps_im
    prod_im = sig_re * taps_im + sig_im * taps_re
    conv = inverse(prod_re, prod_im, tables)
    gain = lax.dynamic_slice_in_dim(skip_gain[0], c_index * chan_width + q_index * own, own)
    gated = (queries * (conv + gain[:, None] * signal)).astype(jnp.bfloat16)

    gated = gated.reshape(own, n_pos, block_rows).transpose(1, 0, 2)
    gated = lax.all_to_all(gated, ("seq", "chan"), 0, 0, tiled=True)
    gated = gated.reshape(n_seq, n_chan, own, block_rows).transpose(3, 1, 0, 2)
    return gated.reshape(block_rows, width)[None]


def solution(mesh):
    in_specs = (
        P("section", "seq", "chan"),
        P("section", "chan", None),
        P("section", ("seq", "chan"), None),
        P("section", None),
    )
    out_specs = P("section", ("seq", "chan"), None)
    return jax.shard_map(body, mesh=mesh, in_specs=in_specs, out_specs=out_specs, check_vma=False)
```

```python
import math

import numpy as np
import jax
import jax.numpy as jnp
from jax import lax
from jax.sharding import PartitionSpec as P


CHUNKS = 2
HI = lax.Precision.HIGH


def dft_tables(seq_len):
    fft_length = 2 * seq_len
    side = int(round(math.sqrt(fft_length)))
    half = seq_len // side
    k = np.arange(side)
    m = np.arange(half)
    outer = 2 * np.pi * np.outer(k, m) / side
    fine = 2 * np.pi * (np.outer(k, k) % side) / side
    twist = 2 * np.pi * (np.outer(k, k) % fft_length) / fft_length
    f32 = lambda a: jnp.asarray(a, dtype=jnp.float32)
    return dict(
        side=side, half=half,
        a_cos=f32(np.cos(outer)), a_sin=f32(np.sin(outer)),
        c_cos=f32(np.cos(fine)), c_sin=f32(np.sin(fine)),
        t_cos=f32(np.cos(twist)), t_sin=f32(np.sin(twist)),
        i_cos=f32(np.cos(outer) / fft_length), i_sin=f32(np.sin(outer) / fft_length),
    )


def forward(x, t):
    c = x.shape[0]
    x = x.reshape(c, t["half"], t["side"])
    y_re = jnp.einsum("km,cmr->ckr", t["a_cos"], x, precision=HI)
    y_im = -jnp.einsum("km,cmr->ckr", t["a_sin"], x, precision=HI)
    z_re = y_re * t["t_cos"] + y_im * t["t_sin"]
    z_im = y_im * t["t_cos"] - y_re * t["t_sin"]
    s_re = jnp.einsum("ckr,rj->ckj", z_re, t["c_cos"], precision=HI) + jnp.einsum("ckr,rj->ckj", z_im, t["c_sin"], precision=HI)
    s_im = jnp.einsum("ckr,rj->ckj", z_im, t["c_cos"], precision=HI) - jnp.einsum("ckr,rj->ckj", z_re, t["c_sin"], precision=HI)
    return s_re, s_im


def inverse(p_re, p_im, t):
    c = p_re.shape[0]
    u_re = jnp.einsum("ckj,jr->ckr", p_re, t["c_cos"], precision=HI) - jnp.einsum("ckj,jr->ckr", p_im, t["c_sin"], precision=HI)
    u_im = jnp.einsum("ckj,jr->ckr", p_im, t["c_cos"], precision=HI) + jnp.einsum("ckj,jr->ckr", p_re, t["c_sin"], precision=HI)
    v_re = u_re * t["t_cos"] - u_im * t["t_sin"]
    v_im = u_im * t["t_cos"] + u_re * t["t_sin"]
    out = jnp.einsum("km,ckr->cmr", t["i_cos"], v_re, precision=HI) - jnp.einsum("km,ckr->cmr", t["i_sin"], v_im, precision=HI)
    return out.reshape(c, -1)


def from_behind(value, axis, steps):
    count = lax.axis_size(axis)
    pairs = [(source, (source + steps) % count) for source in range(count)]
    return lax.ppermute(value, axis, pairs)


def ring_reduce_scatter(partial):
    count = lax.axis_size("chan")
    me = lax.axis_index("chan")
    blocks = partial.reshape(count, partial.shape[0] // count, partial.shape[1])
    half = partial.shape[1] // 2
    right = [(i, (i + 1) % count) for i in range(count)]
    left = [(i, (i - 1) % count) for i in range(count)]

    def pick(index, lo):
        block = lax.dynamic_index_in_dim(blocks, index % count, axis=0, keepdims=False)
        return block[:, half:] if lo else block[:, :half]

    ahead = pick(me - 1, False)
    behind = pick(me + 1, True)
    for step in range(2, count + 1):
        ahead = lax.ppermute(ahead, "chan", right) + pick(me - step, False)
        behind = lax.ppermute(behind, "chan", left) + pick(me + step, True)
    return jnp.concatenate([ahead, behind], axis=1)


def to_owner(value, shift):
    sections = lax.axis_size("section")
    count = lax.axis_size("seq")
    pairs = [
        (s * count + q, ((s + 1) % sections) * count + (q + shift) % count)
        for s in range(sections)
        for q in range(count)
    ]
    return lax.ppermute(value, ("section", "seq"), pairs)


def body(layer_rows, in_weight, long_filter, skip_gain):
    n_chan = lax.axis_size("chan")
    n_seq = lax.axis_size("seq")
    n_pos = n_chan * n_seq
    width = long_filter.shape[2]
    block_rows = long_filter.shape[1]
    seq_rows = layer_rows.shape[1]
    seq_len = block_rows * n_pos
    chan_width = width // n_chan
    own = chan_width // n_seq
    q_index = lax.axis_index("seq")
    c_index = lax.axis_index("chan")

    tables = dft_tables(seq_len)

    taps = long_filter[0].reshape(block_rows, n_chan, n_seq, own)
    taps = taps.transpose(2, 1, 3, 0).reshape(n_pos, own, block_rows)
    taps = lax.all_to_all(taps, ("seq", "chan"), 0, 0, tiled=True)
    taps = taps.reshape(n_pos, own, block_rows).transpose(1, 0, 2).reshape(own, seq_len)
    taps_re, taps_im = forward(taps, tables)

    weight = in_weight[0].reshape(-1, 3, n_chan, n_seq, own)
    weight = jnp.concatenate([weight, weight], axis=3)
    weight = lax.dynamic_slice_in_dim(weight, q_index, n_seq, axis=3)
    weight = weight.transpose(0, 2, 1, 3, 4)
    rows = layer_rows[0]
    arrived = [None] * n_seq
    shifts = n_seq // CHUNKS
    for chunk in range(CHUNKS):
        part = weight[:, :, :, chunk * shifts : (chunk + 1) * shifts].reshape(-1, 3 * n_chan * shifts * own)
        part = from_behind(part, "section", -1)
        partial = jnp.einsum("fn,rf->nr", part, rows, preferred_element_type=jnp.float32)
        if chunk == CHUNKS - 1:
            summed = ring_reduce_scatter(partial)
        else:
            summed = lax.psum_scatter(partial, "chan", scatter_dimension=0, tiled=True)
        summed = summed.astype(jnp.bfloat16).reshape(3, shifts, own, seq_rows)
        for step in range(shifts):
            shift = chunk * shifts + step
            arrived[shift] = to_owner(summed[:, step], shift)
    stacked = jnp.stack(arrived[::-1])
    stacked = jnp.concatenate([stacked, stacked], axis=0)
    mixed = lax.dynamic_slice_in_dim(stacked, n_seq - 1 - q_index, n_seq, axis=0)
    mixed = mixed.transpose(1, 2, 0, 3).reshape(3, own, seq_len)
    queries = mixed[0].astype(jnp.float32)
    signal = mixed[1].astype(jnp.float32) * mixed[2].astype(jnp.float32)

    sig_re, sig_im = forward(signal, tables)
    prod_re = sig_re * taps_re - sig_im * taps_im
    prod_im = sig_re * taps_im + sig_im * taps_re
    conv = inverse(prod_re, prod_im, tables)
    gain = lax.dynamic_slice_in_dim(skip_gain[0], c_index * chan_width + q_index * own, own)
    gated = (queries * (conv + gain[:, None] * signal)).astype(jnp.bfloat16)

    gated = gated.reshape(own, n_pos, block_rows).transpose(1, 0, 2)
    gated = lax.all_to_all(gated, ("seq", "chan"), 0, 0, tiled=True)
    gated = gated.reshape(n_seq, n_chan, own, block_rows).transpose(3, 1, 0, 2)
    return gated.reshape(block_rows, width)[None]


def solution(mesh):
    in_specs = (
        P("section", "seq", "chan"),
        P("section", "chan", None),
        P("section", ("seq", "chan"), None),
        P("section", None),
    )
    out_specs = P("section", ("seq", "chan"), None)
    return jax.shard_map(body, mesh=mesh, in_specs=in_specs, out_specs=out_specs, check_vma=False)
```

```python
import math

import numpy as np
import jax
import jax.numpy as jnp
from jax import lax
from jax.sharding import PartitionSpec as P


CHUNKS = 2
HI = lax.Precision.HIGH


def dft_tables(seq_len):
    fft_length = 2 * seq_len
    side = int(round(math.sqrt(fft_length)))
    half = seq_len // side
    k = np.arange(side)
    m = np.arange(half)
    outer = 2 * np.pi * np.outer(k, m) / side
    fine = 2 * np.pi * (np.outer(k, k) % side) / side
    twist = 2 * np.pi * (np.outer(k, k) % fft_length) / fft_length
    f32 = lambda a: jnp.asarray(a, dtype=jnp.float32)
    return dict(
        side=side, half=half,
        a_cos=f32(np.cos(outer)), a_sin=f32(np.sin(outer)),
        c_cos=f32(np.cos(fine)), c_sin=f32(np.sin(fine)),
        t_cos=f32(np.cos(twist)), t_sin=f32(np.sin(twist)),
        i_cos=f32(np.cos(outer) / fft_length), i_sin=f32(np.sin(outer) / fft_length),
    )


def forward(x, t):
    c = x.shape[0]
    x = x.reshape(c, t["half"], t["side"])
    y_re = jnp.einsum("km,cmr->ckr", t["a_cos"], x, precision=HI)
    y_im = -jnp.einsum("km,cmr->ckr", t["a_sin"], x, precision=HI)
    z_re = y_re * t["t_cos"] + y_im * t["t_sin"]
    z_im = y_im * t["t_cos"] - y_re * t["t_sin"]
    s_re = jnp.einsum("ckr,rj->ckj", z_re, t["c_cos"], precision=HI) + jnp.einsum("ckr,rj->ckj", z_im, t["c_sin"], precision=HI)
    s_im = jnp.einsum("ckr,rj->ckj", z_im, t["c_cos"], precision=HI) - jnp.einsum("ckr,rj->ckj", z_re, t["c_sin"], precision=HI)
    return s_re, s_im


def inverse(p_re, p_im, t):
    c = p_re.shape[0]
    u_re = jnp.einsum("ckj,jr->ckr", p_re, t["c_cos"], precision=HI) - jnp.einsum("ckj,jr->ckr", p_im, t["c_sin"], precision=HI)
    u_im = jnp.einsum("ckj,jr->ckr", p_im, t["c_cos"], precision=HI) + jnp.einsum("ckj,jr->ckr", p_re, t["c_sin"], precision=HI)
    v_re = u_re * t["t_cos"] - u_im * t["t_sin"]
    v_im = u_im * t["t_cos"] + u_re * t["t_sin"]
    out = jnp.einsum("km,ckr->cmr", t["i_cos"], v_re, precision=HI) - jnp.einsum("km,ckr->cmr", t["i_sin"], v_im, precision=HI)
    return out.reshape(c, -1)


def from_behind(value, axis, steps):
    count = lax.axis_size(axis)
    pairs = [(source, (source + steps) % count) for source in range(count)]
    return lax.ppermute(value, axis, pairs)


def exchange_sum(partial):
    count = lax.axis_size("chan")
    blocks = partial.reshape(count, partial.shape[0] // count, partial.shape[1])
    blocks = lax.all_to_all(blocks, "chan", 0, 0, tiled=True)
    return jnp.sum(blocks, axis=0)


def to_owner(value, shift):
    sections = lax.axis_size("section")
    count = lax.axis_size("seq")
    pairs = [
        (s * count + q, ((s + 1) % sections) * count + (q + shift) % count)
        for s in range(sections)
        for q in range(count)
    ]
    return lax.ppermute(value, ("section", "seq"), pairs)


def body(layer_rows, in_weight, long_filter, skip_gain):
    n_chan = lax.axis_size("chan")
    n_seq = lax.axis_size("seq")
    n_pos = n_chan * n_seq
    width = long_filter.shape[2]
    block_rows = long_filter.shape[1]
    seq_rows = layer_rows.shape[1]
    seq_len = block_rows * n_pos
    chan_width = width // n_chan
    own = chan_width // n_seq
    q_index = lax.axis_index("seq")
    c_index = lax.axis_index("chan")

    tables = dft_tables(seq_len)

    taps = long_filter[0].reshape(block_rows, n_chan, n_seq, own)
    taps = taps.transpose(2, 1, 3, 0).reshape(n_pos, own, block_rows)
    taps = lax.all_to_all(taps, ("seq", "chan"), 0, 0, tiled=True)
    taps = taps.reshape(n_pos, own, block_rows).transpose(1, 0, 2).reshape(own, seq_len)
    taps_re, taps_im = forward(taps, tables)

    weight = in_weight[0].reshape(-1, 3, n_chan, n_seq, own)
    weight = jnp.concatenate([weight, weight], axis=3)
    weight = lax.dynamic_slice_in_dim(weight, q_index, n_seq, axis=3)
    weight = weight.transpose(0, 2, 1, 3, 4)
    rows = layer_rows[0]
    arrived = [None] * n_seq
    shifts = n_seq // CHUNKS
    for chunk in range(CHUNKS):
        part = weight[:, :, :, chunk * shifts : (chunk + 1) * shifts].reshape(-1, 3 * n_chan * shifts * own)
        part = from_behind(part, "section", -1)
        partial = jnp.einsum("fn,rf->nr", part, rows, preferred_element_type=jnp.float32)
        summed = exchange_sum(partial)
        summed = summed.astype(jnp.bfloat16).reshape(3, shifts, own, seq_rows)
        for step in range(shifts):
            shift = chunk * shifts + step
            arrived[shift] = to_owner(summed[:, step], shift)
    stacked = jnp.stack(arrived[::-1])
    stacked = jnp.concatenate([stacked, stacked], axis=0)
    mixed = lax.dynamic_slice_in_dim(stacked, n_seq - 1 - q_index, n_seq, axis=0)
    mixed = mixed.transpose(1, 2, 0, 3).reshape(3, own, seq_len)
    queries = mixed[0].astype(jnp.float32)
    signal = mixed[1].astype(jnp.float32) * mixed[2].astype(jnp.float32)

    sig_re, sig_im = forward(signal, tables)
    prod_re = sig_re * taps_re - sig_im * taps_im
    prod_im = sig_re * taps_im + sig_im * taps_re
    conv = inverse(prod_re, prod_im, tables)
    gain = lax.dynamic_slice_in_dim(skip_gain[0], c_index * chan_width + q_index * own, own)
    gated = (queries * (conv + gain[:, None] * signal)).astype(jnp.bfloat16)

    gated = gated.reshape(own, n_pos, block_rows).transpose(1, 0, 2)
    gated = lax.all_to_all(gated, ("seq", "chan"), 0, 0, tiled=True)
    gated = gated.reshape(n_seq, n_chan, own, block_rows).transpose(3, 1, 0, 2)
    return gated.reshape(block_rows, width)[None]


def solution(mesh):
    in_specs = (
        P("section", "seq", "chan"),
        P("section", "chan", None),
        P("section", ("seq", "chan"), None),
        P("section", None),
    )
    out_specs = P("section", ("seq", "chan"), None)
    return jax.shard_map(body, mesh=mesh, in_specs=in_specs, out_specs=out_specs, check_vma=False)
```
